512 devices in a mesh: req: 8 (over x, core), gx: 8 (over z_lo), gy: 8 (over y, z_hi).
Axes of the slice: x: 4, y: 4, z: 16 (z_hi: 2, z_lo: 8; z = z_hi * 8 + z_lo), core: 2. Of those that a mesh axis runs over, the one named last changes fastest.
Arguments:
- hidden: bfloat16 [6144, 4096], P(('req', 'gx'), 'gy')
- ln_gain: float32 [4096], P('gy'), may hold values from 0.25 to 1.75
- w_qkv: bfloat16 [4096, 32, 384], P('gy', 'gx'), may hold values from -0.09375 to 0.09375
- w_out: bfloat16 [4096, 4096], P('gx', 'gy'), may hold values from -0.375 to 0.375
- kv_cache: bfloat16 [16, 2176, 2, 4096], P('req', 'gy', None, 'gx')
- cache_len: int32 [16], P('req'), may hold values from 0 to 1792, as said below
Outputs:
- mixed: bfloat16 [6144, 4096], P(('req', 'gx'), 'gy')
- cache_out: bfloat16 [16, 2176, 2, 4096], P('req', 'gy', None, 'gx')
The draws below stay inside these ranges and needn't reach their ends.
Inputs may be any that keep to these rules, and one draw needn't show every extreme that they name: `cache_len`: cached lengths are heavy-tailed; some request has exactly 1792.
All inputs are finite; a program needn't handle non-finite values.
Results may differ from the reference program's by a relative error of at most 0.04.
Values may be sent and summed in bfloat16 or wider, within the bound.
No kernel may reach another device: no remote copies, remote signals or barrier semaphores. Data moves between devices by JAX's collectives and lax.ppermute only.
A program may use at most 64 MiB of HBM per device.

```python
import math
import jax
import jax.numpy as jnp
from jax import lax

D = 4096
H = 32
HD = 128
GROUP = 384
PAST = 1792
REQS = 16
TOKENS = 6144
CAP = 2176
N_GY = 8


def draw_hidden(key, part):
    first = jax.random.fold_in(key, 0)
    columns = jnp.arange(D, dtype=jnp.float32)
    column_scale = 1.0 + 2.0 * columns / D
    values = jax.random.normal(first, (TOKENS, D), jnp.float32) * column_scale[None, :]
    return values.astype(jnp.bfloat16)


def draw_kv_cache(key, part):
    first = jax.random.fold_in(key, 0)
    values = jax.random.normal(first, (REQS, CAP, 2, D), jnp.float32)
    return values.astype(jnp.bfloat16)


def draw_cache_len(key, part):
    first, second, third = jax.random.split(key, 3)
    divisor = jax.random.randint(first, (REQS,), 1, 17)
    lengths = jax.random.randint(second, (REQS,), 0, PAST + 1) // divisor
    chosen = jax.random.randint(third, (), 0, REQS)
    lengths = jnp.where(jnp.arange(REQS, dtype=jnp.int32) == chosen, PAST, lengths)
    return lengths.astype(jnp.int32)


def shard_levels(key, shape, cuts, low, high):
    loudness = 1.0
    for axis_at, blocks in cuts:
        heights = jax.random.uniform(jax.random.fold_in(jax.random.fold_in(key, 6), axis_at), (blocks,), jnp.float32, low / len(cuts), high / len(cuts))
        loudness = loudness * jnp.repeat(jnp.exp(heights), shape[axis_at] // blocks).reshape((-1,) + (1,) * (len(shape) - 1 - axis_at))
    return loudness


def noise(own_key, dims, scale, bound, pieces=(), kind=jnp.bfloat16):
    drawn = scale * jax.random.normal(own_key, dims, jnp.float32)
    if pieces:
        drawn = drawn * shard_levels(own_key, dims, pieces, -0.22, 0.18)
    return jnp.clip(drawn, -bound, bound).astype(kind)


def setup_inputs(seed: int = 0) -> dict:
    streams_of = jax.random.split(jax.random.key(seed), 7)
    return {
        "hidden": draw_hidden(jax.random.fold_in(streams_of[6], 71), 0),
        "ln_gain": jnp.clip(1.0 + 0.15 * jax.random.normal(streams_of[1], (D,), jnp.float32), 0.25, 1.75),
        "w_qkv": noise(streams_of[2], (D, H, 3 * HD), D ** -0.5, 0.09375, ((0, 8), (1, 8))),
        "w_out": noise(streams_of[3], (D, D), (D // 16) ** -0.5, 0.375, ((0, 8), (1, 8))),
        "kv_cache": draw_kv_cache(jax.random.fold_in(streams_of[6], 71), 0),
        "cache_len": draw_cache_len(jax.random.fold_in(streams_of[6], 71), 0),
    }


norm_eps = 1e-05
floor_score = -1e+30

def attend(query, keys, values, length, slopes):
    count = query.shape[0]
    places = keys.shape[0]
    scale = 1.0 / math.sqrt(query.shape[2])
    scores = jnp.einsum('chd,phd->chp', query.astype(jnp.float32), keys.astype(jnp.float32)) * scale
    distance = (length + jnp.arange(count, dtype=jnp.int32))[:, None] - jnp.arange(places, dtype=jnp.int32)[None, :]
    valid = distance >= 0
    scores = scores - slopes[None, :, None] * distance.astype(jnp.float32)[:, None, :]
    scores = jnp.where(valid[:, None, :], scores, floor_score)
    highest = lax.optimization_barrier(jnp.max(scores, axis=-1, keepdims=True))
    weights = jnp.where(valid[:, None, :], jnp.exp(scores - highest), 0.0)
    totals = lax.optimization_barrier(jnp.sum(weights, axis=-1))
    rounded = weights.astype(jnp.bfloat16)
    summed = jnp.einsum('chp,phd->chd', rounded.astype(jnp.float32), values.astype(jnp.float32))
    return summed / totals[..., None]

def reference(hidden, ln_gain, w_qkv, w_out, kv_cache, cache_len):
    hidden_f = hidden.astype(jnp.float32)
    mean = lax.optimization_barrier(jnp.mean(hidden_f, axis=1, keepdims=True))
    var = lax.optimization_barrier(jnp.mean(hidden_f * hidden_f, axis=1, keepdims=True)) - mean * mean
    normed = ((hidden_f - mean) * lax.rsqrt(var + norm_eps) * ln_gain[None, :]).astype(jnp.bfloat16)
    flat = w_qkv.reshape(D, 3 * D)
    span = D // N_GY
    summed = jnp.zeros((TOKENS, 3 * D), jnp.float32)
    for block in range(N_GY):
        part = jnp.dot(normed[:, block * span:(block + 1) * span], flat[block * span:(block + 1) * span], preferred_element_type=jnp.float32)
        part = lax.optimization_barrier(part.astype(jnp.bfloat16)).astype(jnp.float32)
        summed = summed + part
    qkv = summed.astype(jnp.bfloat16).reshape(REQS, GROUP, H, 3 * HD)
    slopes = jnp.exp2(-8.0 * (jnp.arange(H, dtype=jnp.int32) + 1).astype(jnp.float32) / H)

    def one_request(items):
        row_qkv, cache, length = items
        query = row_qkv[:, :, :HD]
        fresh = jnp.stack([row_qkv[:, :, HD:2 * HD].reshape(GROUP, D), row_qkv[:, :, 2 * HD:].reshape(GROUP, D)], axis=1)
        offset = jnp.arange(CAP, dtype=jnp.int32) - length
        inside = (offset >= 0) & (offset < GROUP)
        taken = jnp.take(fresh, jnp.clip(offset, 0, GROUP - 1), axis=0)
        updated = jnp.where(inside[:, None, None], taken, cache)
        keys = updated[:, 0].reshape(CAP, H, HD)
        values = updated[:, 1].reshape(CAP, H, HD)
        result = attend(query, keys, values, length, slopes).astype(jnp.bfloat16).reshape(GROUP, D)
        return (result, updated)
    attn, cache_out = lax.map(one_request, (qkv, kv_cache, cache_len))
    mixed = (jnp.dot(attn.reshape(TOKENS, D), w_out, preferred_element_type=jnp.float32) + hidden_f).astype(jnp.bfloat16)
    return (mixed, cache_out)
```

```python
import math

import jax
import jax.numpy as jnp
from jax import lax
from jax.sharding import Mesh
from jax.sharding import PartitionSpec as P

D = 4096


norm_eps = 1e-05
floor_score = -1e30


GY = ("gyy", "gyz")


def gy_index():
    return lax.axis_index("gyy") * lax.axis_size("gyz") + lax.axis_index("gyz")


def gy_sum(x):
    return lax.psum(lax.psum(x, "gyy"), "gyz")


def gy_max(x):
    return lax.pmax(lax.pmax(x, "gyz"), "gyy")


def gy_sum_rows(x, twice):
    part = lax.psum_scatter(x, "gyy", scatter_dimension=0, tiled=True)
    if twice:
        part = lax.psum_scatter(part, "gyz", scatter_dimension=0, tiled=True)
        part = lax.all_gather(part, "gyz", axis=0, tiled=True)
    else:
        part = lax.psum(part, "gyz")
    return lax.all_gather(part, "gyy", axis=0, tiled=True)


def partial_attend(query, keys, values, valid, distance, slopes, scale):
    scores = jnp.einsum("chd,phd->chp", query, keys, preferred_element_type=jnp.float32) * scale
    scores = scores - slopes[None, :, None] * distance.astype(jnp.float32)[:, None, :]
    scores = jnp.where(valid[:, None, :], scores, floor_score)
    highest = jnp.max(scores, axis=-1)
    weights = jnp.where(valid[:, None, :], jnp.exp(scores - highest[..., None]), 0.0)
    totals = jnp.sum(weights, axis=-1)
    accum = jnp.einsum(
        "chp,phd->chd", weights.astype(jnp.bfloat16), values, preferred_element_type=jnp.float32
    )
    return (highest, totals, accum)


def write_cache(fresh_rows, cache_block, positions, length, group):
    offset = positions - length
    inside = (offset >= 0) & (offset < group)
    taken = jnp.take(fresh_rows, jnp.clip(offset, 0, group - 1), axis=0)
    return jnp.where(inside[:, None, None], taken, cache_block)


def shards(hidden, ln_gain, w_qkv, w_out, kv_cache, cache_len):
    hidden_f = hidden.astype(jnp.float32)
    sums = gy_sum((jnp.sum(hidden_f, axis=1), jnp.sum(hidden_f * hidden_f, axis=1)))
    mean = sums[0] / D
    var = sums[1] / D - mean * mean
    normed = (
        (hidden_f - mean[:, None]) * lax.rsqrt(var + norm_eps)[:, None] * ln_gain[None, :]
    ).astype(jnp.bfloat16)
    local_heads = w_qkv.shape[1]
    head_size = w_qkv.shape[2] // 3
    weight_flat = w_qkv.reshape(w_qkv.shape[0], local_heads * 3 * head_size)
    partial_value = jnp.dot(
        lax.all_gather(normed, "gx", axis=0, tiled=True),
        weight_flat,
        preferred_element_type=jnp.float32,
    )
    requests = cache_len.shape[0]
    all_rows = partial_value.shape[0]
    group = all_rows // requests
    width_local = local_heads * head_size
    block = kv_cache.shape[1]
    positions = gy_index() * block + jnp.arange(block, dtype=jnp.int32)
    head_ids = lax.axis_index("gx") * local_heads + jnp.arange(local_heads, dtype=jnp.int32)
    all_heads = local_heads * lax.axis_size("gx")
    slopes = jnp.exp2(-8.0 * (head_ids + 1).astype(jnp.float32) / all_heads)
    scale = 1.0 / math.sqrt(head_size)
    steps_c = jnp.arange(group, dtype=jnp.int32)
    tops_list = []
    totals_list = []
    accum_list = []
    caches = []
    qkv = gy_sum_rows(partial_value.astype(jnp.bfloat16), True)
    qkv = qkv.reshape(requests, group, local_heads, 3 * head_size)
    fresh = jnp.stack(
        [
            qkv[:, :, :, head_size : 2 * head_size].reshape(requests, group, width_local),
            qkv[:, :, :, 2 * head_size :].reshape(requests, group, width_local),
        ],
        axis=2,
    )
    for request in range(requests):
        length = cache_len[request]
        updated = write_cache(fresh[request], kv_cache[request], positions, length, group)
        caches.append(updated)
        keys = updated[:, 0].reshape(block, local_heads, head_size)
        values = updated[:, 1].reshape(block, local_heads, head_size)
        distance = (length + steps_c)[:, None] - positions[None, :]
        part_top, part_total, part_accum = partial_attend(
            qkv[request, :, :, :head_size], keys, values, distance >= 0, distance, slopes, scale
        )
        tops_list.append(part_top)
        totals_list.append(part_total)
        accum_list.append(part_accum)
    tops = jnp.stack(tops_list)
    totals = jnp.stack(totals_list)
    accums = jnp.stack(accum_list)
    overall = gy_max(tops)
    factor = jnp.exp(tops - overall)
    rows = requests * group
    packed = jnp.concatenate(
        [
            (accums * factor[..., None]).astype(jnp.bfloat16).reshape(rows, width_local),
            (totals * factor).astype(jnp.bfloat16).reshape(rows, local_heads),
        ],
        axis=1,
    )
    packed = gy_sum_rows(packed, False).astype(jnp.float32)
    joined_accums = packed[:, :width_local].reshape(accums.shape)
    joined_totals = packed[:, width_local:].reshape(totals.shape)
    attn = (
        (joined_accums / joined_totals[..., None])
        .astype(jnp.bfloat16)
        .reshape(requests * group, width_local)
    )
    projected = lax.psum_scatter(
        jnp.dot(attn, w_out, preferred_element_type=jnp.float32).astype(jnp.bfloat16),
        "gx",
        scatter_dimension=0,
        tiled=True,
    ).astype(jnp.float32)
    mixed = (projected + hidden_f).astype(jnp.bfloat16)
    return (mixed, jnp.stack(caches))


def solution(mesh):
    n_gy = mesh.shape["gy"]
    split = Mesh(
        mesh.devices.reshape(mesh.shape["req"], mesh.shape["gx"], n_gy // 2, 2),
        ("req", "gx") + GY,
    )
    in_specs = (
        P(("req", "gx"), GY),
        P(GY),
        P(GY, "gx", None),
        P("gx", GY),
        P("req", GY, None, "gx"),
        P("req"),
    )
    out_specs = (P(("req", "gx"), GY), P("req", GY, None, "gx"))
    return jax.shard_map(shards, mesh=split, in_specs=in_specs, out_specs=out_specs, check_vma=False)
```

```python
import math

import jax
import jax.numpy as jnp
from jax import lax
from jax.sharding import Mesh
from jax.sharding import PartitionSpec as P

D = 4096


norm_eps = 1e-05
floor_score = -1e30


GY = ("gyy", "gyz")


def gy_index():
    return lax.axis_index("gyy") * lax.axis_size("gyz") + lax.axis_index("gyz")


def shift(x, axis, step):
    n = lax.axis_size(axis)
    return lax.ppermute(x, axis, [(i, (i + step) % n) for i in range(n)])


def swap_combine(x, axis, op):
    wide = x.astype(jnp.float32) if op is jnp.add else x
    total = wide
    for step in range(1, lax.axis_size(axis)):
        total = op(total, shift(x, axis, step).astype(wide.dtype))
    return total


def ring_scatter_sum(x, axis):
    n = lax.axis_size(axis)
    me = lax.axis_index(axis)
    rows = x.shape[0] // n
    total = lax.dynamic_slice_in_dim(x, me * rows, rows).astype(jnp.float32)
    for step in range(1, n):
        block = lax.dynamic_slice_in_dim(x, ((me + step) % n) * rows, rows)
        total = total + shift(block, axis, step).astype(jnp.float32)
    return total


def ring_gather(x, axis):
    n = lax.axis_size(axis)
    me = lax.axis_index(axis)
    stacked = jnp.stack([x] + [shift(x, axis, step) for step in range(1, n)])
    order = (me - jnp.arange(n, dtype=jnp.int32)) % n
    taken = jnp.take(stacked, order, axis=0)
    return taken.reshape((n * x.shape[0],) + x.shape[1:])


def gy_sum(x):
    return swap_combine(swap_combine(x, "gyz", jnp.add), "gyy", jnp.add)


def gy_max(x):
    return swap_combine(swap_combine(x, "gyz", jnp.maximum), "gyy", jnp.maximum)


def gy_sum_rows(x):
    part = ring_scatter_sum(x, "gyy").astype(x.dtype)
    part = swap_combine(part, "gyz", jnp.add).astype(x.dtype)
    return ring_gather(part, "gyy")


def partial_attend(query, keys, values, valid, distance, slopes, scale):
    scores = jnp.einsum("chd,phd->chp", query, keys, preferred_element_type=jnp.float32) * scale
    scores = scores - slopes[None, :, None] * distance.astype(jnp.float32)[:, None, :]
    scores = jnp.where(valid[:, None, :], scores, floor_score)
    highest = jnp.max(scores, axis=-1)
    weights = jnp.where(valid[:, None, :], jnp.exp(scores - highest[..., None]), 0.0)
    totals = jnp.sum(weights, axis=-1)
    accum = jnp.einsum(
        "chp,phd->chd", weights.astype(jnp.bfloat16), values, preferred_element_type=jnp.float32
    )
    return (highest, totals, accum)


def write_cache(fresh_rows, cache_block, positions, length, group):
    offset = positions - length
    inside = (offset >= 0) & (offset < group)
    taken = jnp.take(fresh_rows, jnp.clip(offset, 0, group - 1), axis=0)
    return jnp.where(inside[:, None, None], taken, cache_block)


def shards(hidden, ln_gain, w_qkv, w_out, kv_cache, cache_len):
    hidden_f = hidden.astype(jnp.float32)
    sums = gy_sum(jnp.stack([jnp.sum(hidden_f, axis=1), jnp.sum(hidden_f * hidden_f, axis=1)]))
    mean = sums[0] / D
    var = sums[1] / D - mean * mean
    normed = (
        (hidden_f - mean[:, None]) * lax.rsqrt(var + norm_eps)[:, None] * ln_gain[None, :]
    ).astype(jnp.bfloat16)
    local_heads = w_qkv.shape[1]
    head_size = w_qkv.shape[2] // 3
    weight_flat = w_qkv.reshape(w_qkv.shape[0], local_heads * 3 * head_size)
    partial_value = jnp.dot(
        ring_gather(normed, "gx"),
        weight_flat,
        preferred_element_type=jnp.float32,
    )
    requests = cache_len.shape[0]
    all_rows = partial_value.shape[0]
    group = all_rows // requests
    width_local = local_heads * head_size
    block = kv_cache.shape[1]
    positions = gy_index() * block + jnp.arange(block, dtype=jnp.int32)
    head_ids = lax.axis_index("gx") * local_heads + jnp.arange(local_heads, dtype=jnp.int32)
    all_heads = local_heads * lax.axis_size("gx")
    slopes = jnp.exp2(-8.0 * (head_ids + 1).astype(jnp.float32) / all_heads)
    scale = 1.0 / math.sqrt(head_size)
    steps_c = jnp.arange(group, dtype=jnp.int32)
    tops_list = []
    totals_list = []
    accum_list = []
    caches = []
    qkv = gy_sum_rows(partial_value.astype(jnp.bfloat16))
    qkv = qkv.reshape(requests, group, local_heads, 3 * head_size)
    fresh = jnp.stack(
        [
            qkv[:, :, :, head_size : 2 * head_size].reshape(requests, group, width_local),
            qkv[:, :, :, 2 * head_size :].reshape(requests, group, width_local),
        ],
        axis=2,
    )
    for request in range(requests):
        length = cache_len[request]
        updated = write_cache(fresh[request], kv_cache[request], positions, length, group)
        caches.append(updated)
        keys = updated[:, 0].reshape(block, local_heads, head_size)
        values = updated[:, 1].reshape(block, local_heads, head_size)
        distance = (length + steps_c)[:, None] - positions[None, :]
        part_top, part_total, part_accum = partial_attend(
            qkv[request, :, :, :head_size], keys, values, distance >= 0, distance, slopes, scale
        )
        tops_list.append(part_top)
        totals_list.append(part_total)
        accum_list.append(part_accum)
    tops = jnp.stack(tops_list)
    totals = jnp.stack(totals_list)
    accums = jnp.stack(accum_list)
    overall = gy_max(tops)
    factor = jnp.exp(tops - overall)
    rows = requests * group
    packed = jnp.concatenate(
        [
            (accums * factor[..., None]).astype(jnp.bfloat16).reshape(rows, width_local),
            (totals * factor).astype(jnp.bfloat16).reshape(rows, local_heads),
        ],
        axis=1,
    )
    packed = gy_sum_rows(packed).astype(jnp.float32)
    joined_accums = packed[:, :width_local].reshape(accums.shape)
    joined_totals = packed[:, width_local:].reshape(totals.shape)
    attn = (
        (joined_accums / joined_totals[..., None])
        .astype(jnp.bfloat16)
        .reshape(requests * group, width_local)
    )
    projected = ring_scatter_sum(
        jnp.dot(attn, w_out, preferred_element_type=jnp.float32).astype(jnp.bfloat16), "gx"
    )
    mixed = (projected + hidden_f).astype(jnp.bfloat16)
    return (mixed, jnp.stack(caches))


def solution(mesh):
    n_gy = mesh.shape["gy"]
    split = Mesh(
        mesh.devices.reshape(mesh.shape["req"], mesh.shape["gx"], n_gy // 2, 2),
        ("req", "gx") + GY,
    )
    in_specs = (
        P(("req", "gx"), GY),
        P(GY),
        P(GY, "gx", None),
        P("gx", GY),
        P("req", GY, None, "gx"),
        P("req"),
    )
    out_specs = (P(("req", "gx"), GY), P("req", GY, None, "gx"))
    return jax.shard_map(shards, mesh=split, in_specs=in_specs, out_specs=out_specs, check_vma=False)
```

```python
import math

import jax
import jax.numpy as jnp
from jax import lax
from jax.sharding import Mesh
from jax.sharding import PartitionSpec as P

D = 4096


norm_eps = 1e-05
floor_score = -1e30


GY = ("gyy", "gyz")


def gy_index():
    return lax.axis_index("gyy") * lax.axis_size("gyz") + lax.axis_index("gyz")


def shift(x, axis, step):
    n = lax.axis_size(axis)
    return lax.ppermute(x, axis, [(i, (i + step) % n) for i in range(n)])


def swap_combine(x, axis, op):
    wide = x.astype(jnp.float32) if op is jnp.add else x
    total = wide
    for step in range(1, lax.axis_size(axis)):
        total = op(total, shift(x, axis, step).astype(wide.dtype))
    return total


def ring_scatter_sum(x, axis):
    n = lax.axis_size(axis)
    me = lax.axis_index(axis)
    rows = x.shape[0] // n
    total = lax.dynamic_slice_in_dim(x, me * rows, rows).astype(jnp.float32)
    for step in range(1, n):
        block = lax.dynamic_slice_in_dim(x, ((me + step) % n) * rows, rows)
        total = total + shift(block, axis, step).astype(jnp.float32)
    return total


def ring_gather(x, axis):
    n = lax.axis_size(axis)
    me = lax.axis_index(axis)
    stacked = jnp.stack([x] + [shift(x, axis, step) for step in range(1, n)])
    order = (me - jnp.arange(n, dtype=jnp.int32)) % n
    taken = jnp.take(stacked, order, axis=0)
    return taken.reshape((n * x.shape[0],) + x.shape[1:])


def merge(parts, heads):
    top = parts[0][1]
    for _, high in parts[1:]:
        top = jnp.maximum(top, high)
    total = 0.0
    for block, high in parts:
        factor = jnp.exp(high - top)
        wide = jnp.repeat(factor, block.shape[1] // heads - 1, axis=1)
        total = total + block.astype(jnp.float32) * jnp.concatenate([wide, factor], axis=1)
    return total, top


def attend_combine(packed, tops, heads):
    n = lax.axis_size("gyy")
    me = lax.axis_index("gyy")
    rows = packed.shape[0] // n
    parts = []
    for step in range(n):
        block = lax.dynamic_slice_in_dim(packed, ((me + step) % n) * rows, rows)
        high = lax.dynamic_slice_in_dim(tops, ((me + step) % n) * rows, rows)
        parts.append((block, high) if step == 0 else shift((block, high), "gyy", step))
    total, top = merge(parts, heads)
    own = (total.astype(packed.dtype), top)
    total, _ = merge([own, shift(own, "gyz", 1)], heads)
    width = total.shape[1] - heads
    sums = total[:, :width].reshape(rows, heads, width // heads)
    attn = (sums / total[:, width:, None]).astype(packed.dtype).reshape(rows, width)
    return ring_gather(attn, "gyy")


def gy_sum(x):
    return swap_combine(swap_combine(x, "gyz", jnp.add), "gyy", jnp.add)


def gy_max(x):
    return swap_combine(swap_combine(x, "gyz", jnp.maximum), "gyy", jnp.maximum)


def gy_sum_rows(x):
    part = ring_scatter_sum(x, "gyy").astype(x.dtype)
    part = swap_combine(part, "gyz", jnp.add).astype(x.dtype)
    return ring_gather(part, "gyy")


def partial_attend(query, keys, values, valid, distance, slopes, scale):
    scores = jnp.einsum("chd,phd->chp", query, keys, preferred_element_type=jnp.float32) * scale
    scores = scores - slopes[None, :, None] * distance.astype(jnp.float32)[:, None, :]
    scores = jnp.where(valid[:, None, :], scores, floor_score)
    highest = jnp.max(scores, axis=-1)
    weights = jnp.where(valid[:, None, :], jnp.exp(scores - highest[..., None]), 0.0)
    totals = jnp.sum(weights, axis=-1)
    accum = jnp.einsum(
        "chp,phd->chd", weights.astype(jnp.bfloat16), values, preferred_element_type=jnp.float32
    )
    return (highest, totals, accum)


def write_cache(fresh_rows, cache_block, positions, length, group):
    offset = positions - length
    inside = (offset >= 0) & (offset < group)
    taken = jnp.take(fresh_rows, jnp.clip(offset, 0, group - 1), axis=0)
    return jnp.where(inside[:, None, None], taken, cache_block)


def shards(hidden, ln_gain, w_qkv, w_out, kv_cache, cache_len):
    hidden_f = hidden.astype(jnp.float32)
    gathered = ring_gather(hidden, "gx").astype(jnp.float32)
    sums = gy_sum(jnp.stack([jnp.sum(hidden_f, axis=1), jnp.sum(hidden_f * hidden_f, axis=1)], axis=1))
    sums = ring_gather(sums, "gx")
    mean = sums[:, 0] / D
    var = sums[:, 1] / D - mean * mean
    normed = (
        (gathered - mean[:, None]) * lax.rsqrt(var + norm_eps)[:, None] * ln_gain[None, :]
    ).astype(jnp.bfloat16)
    local_heads = w_qkv.shape[1]
    head_size = w_qkv.shape[2] // 3
    weight_flat = w_qkv.reshape(w_qkv.shape[0], local_heads * 3 * head_size)
    partial_value = jnp.dot(
        normed,
        weight_flat,
        preferred_element_type=jnp.float32,
    )
    requests = cache_len.shape[0]
    all_rows = partial_value.shape[0]
    group = all_rows // requests
    width_local = local_heads * head_size
    block = kv_cache.shape[1]
    positions = gy_index() * block + jnp.arange(block, dtype=jnp.int32)
    head_ids = lax.axis_index("gx") * local_heads + jnp.arange(local_heads, dtype=jnp.int32)
    all_heads = local_heads * lax.axis_size("gx")
    slopes = jnp.exp2(-8.0 * (head_ids + 1).astype(jnp.float32) / all_heads)
    scale = 1.0 / math.sqrt(head_size)
    steps_c = jnp.arange(group, dtype=jnp.int32)
    tops_list = []
    totals_list = []
    accum_list = []
    caches = []
    qkv = gy_sum_rows(partial_value.astype(jnp.bfloat16))
    qkv = qkv.reshape(requests, group, local_heads, 3 * head_size)
    fresh = jnp.stack(
        [
            qkv[:, :, :, head_size : 2 * head_size].reshape(requests, group, width_local),
            qkv[:, :, :, 2 * head_size :].reshape(requests, group, width_local),
        ],
        axis=2,
    )
    for request in range(requests):
        length = cache_len[request]
        updated = write_cache(fresh[request], kv_cache[request], positions, length, group)
        caches.append(updated)
        keys = updated[:, 0].reshape(block, local_heads, head_size)
        values = updated[:, 1].reshape(block, local_heads, head_size)
        distance = (length + steps_c)[:, None] - positions[None, :]
        part_top, part_total, part_accum = partial_attend(
            qkv[request, :, :, :head_size], keys, values, distance >= 0, distance, slopes, scale
        )
        tops_list.append(part_top)
        totals_list.append(part_total)
        accum_list.append(part_accum)
    tops = jnp.stack(tops_list)
    totals = jnp.stack(totals_list)
    accums = jnp.stack(accum_list)
    rows = requests * group
    packed = jnp.concatenate(
        [
            accums.astype(jnp.bfloat16).reshape(rows, width_local),
            totals.astype(jnp.bfloat16).reshape(rows, local_heads),
        ],
        axis=1,
    )
    attn = attend_combine(packed, tops.reshape(rows, local_heads), local_heads)
    projected = ring_scatter_sum(
        jnp.dot(attn, w_out, preferred_element_type=jnp.float32).astype(jnp.bfloat16), "gx"
    )
    mixed = (projected + hidden_f).astype(jnp.bfloat16)
    return (mixed, jnp.stack(caches))


def solution(mesh):
    n_gy = mesh.shape["gy"]
    split = Mesh(
        mesh.devices.reshape(mesh.shape["req"], mesh.shape["gx"], n_gy // 2, 2),
        ("req", "gx") + GY,
    )
    in_specs = (
        P(("req", "gx"), GY),
        P(GY),
        P(GY, "gx", None),
        P("gx", GY),
        P("req", GY, None, "gx"),
        P("req"),
    )
    out_specs = (P(("req", "gx"), GY), P("req", GY, None, "gx"))
    return jax.shard_map(shards, mesh=split, in_specs=in_specs, out_specs=out_specs, check_vma=False)
```

```python
import math

import jax
import jax.numpy as jnp
from jax import lax
from jax.sharding import Mesh
from jax.sharding import PartitionSpec as P

D = 4096


norm_eps = 1e-05
floor_score = -1e30


GY = ("gyy", "gyz")


def gy_index():
    return lax.axis_index("gyy") * lax.axis_size("gyz") + lax.axis_index("gyz")


def shift(x, axis, step):
    n = lax.axis_size(axis)
    return lax.ppermute(x, axis, [(i, (i + step) % n) for i in range(n)])


def swap_combine(x, axis, op):
    wide = x.astype(jnp.float32) if op is jnp.add else x
    total = wide
    for step in range(1, lax.axis_size(axis)):
        total = op(total, shift(x, axis, step).astype(wide.dtype))
    return total


def ring_scatter_sum(x, axis):
    n = lax.axis_size(axis)
    me = lax.axis_index(axis)
    rows = x.shape[0] // n
    total = lax.dynamic_slice_in_dim(x, me * rows, rows).astype(jnp.float32)
    for step in range(1, n):
        block = lax.dynamic_slice_in_dim(x, ((me + step) % n) * rows, rows)
        total = total + shift(block, axis, step).astype(jnp.float32)
    return total


def ring_gather(x, axis):
    n = lax.axis_size(axis)
    me = lax.axis_index(axis)
    stacked = jnp.stack([x] + [shift(x, axis, step) for step in range(1, n)])
    order = (me - jnp.arange(n, dtype=jnp.int32)) % n
    taken = jnp.take(stacked, order, axis=0)
    return taken.reshape((n * x.shape[0],) + x.shape[1:])


def split3(x):
    pieces = []
    for _ in range(3):
        piece = x.astype(jnp.bfloat16)
        pieces.append(piece)
        x = x - piece.astype(jnp.float32)
    return jnp.concatenate(pieces, axis=1)


def join3(x, heads):
    wide = x.astype(jnp.float32)
    return wide[:, :heads] + wide[:, heads : 2 * heads] + wide[:, 2 * heads :]


def merge(parts, heads):
    parts = [(block[:, : -3 * heads], join3(block[:, -3 * heads :], heads)) for block in parts]
    top = parts[0][1]
    for _, high in parts[1:]:
        top = jnp.maximum(top, high)
    total = 0.0
    for block, high in parts:
        factor = jnp.exp(high - top)
        wide = jnp.repeat(factor, block.shape[1] // heads - 1, axis=1)
        total = total + block.astype(jnp.float32) * jnp.concatenate([wide, factor], axis=1)
    return total, top


def attend_combine(packed, tops, heads):
    n = lax.axis_size("gyy")
    me = lax.axis_index("gyy")
    rows = packed.shape[0] // n
    packed = jnp.concatenate([packed, split3(tops)], axis=1)
    parts = []
    for step in range(n):
        block = lax.dynamic_slice_in_dim(packed, ((me + step) % n) * rows, rows)
        parts.append(block if step == 0 else shift(block, "gyy", step))
    total, top = merge(parts, heads)
    own = jnp.concatenate([total.astype(packed.dtype), split3(top)], axis=1)
    total, _ = merge([own, shift(own, "gyz", 1)], heads)
    width = total.shape[1] - heads
    sums = total[:, :width].reshape(rows, heads, width // heads)
    attn = (sums / total[:, width:, None]).astype(packed.dtype).reshape(rows, width)
    return ring_gather(attn, "gyy")


def gy_sum(x):
    return swap_combine(swap_combine(x, "gyz", jnp.add), "gyy", jnp.add)


def gy_max(x):
    return swap_combine(swap_combine(x, "gyz", jnp.maximum), "gyy", jnp.maximum)


def exchange_scatter_sum(x, axis):
    n = lax.axis_size(axis)
    split = x.reshape((n, x.shape[0] // n) + x.shape[1:])
    return jnp.sum(lax.all_to_all(split, axis, 0, 0).astype(jnp.float32), axis=0)


def exchange_gather(x, axis):
    n = lax.axis_size(axis)
    copies = jnp.broadcast_to(x[None], (n,) + x.shape)
    return lax.all_to_all(copies, axis, 0, 0).reshape((n * x.shape[0],) + x.shape[1:])


def gy_sum_rows(x):
    part = exchange_scatter_sum(x, "gyy").astype(x.dtype)
    part = swap_combine(part, "gyz", jnp.add).astype(x.dtype)
    return exchange_gather(part, "gyy")


def partial_attend(query, keys, values, valid, distance, slopes, scale):
    scores = jnp.einsum("chd,phd->chp", query, keys, preferred_element_type=jnp.float32) * scale
    scores = scores - slopes[None, :, None] * distance.astype(jnp.float32)[:, None, :]
    scores = jnp.where(valid[:, None, :], scores, floor_score)
    highest = jnp.max(scores, axis=-1)
    weights = jnp.where(valid[:, None, :], jnp.exp(scores - highest[..., None]), 0.0)
    totals = jnp.sum(weights, axis=-1)
    accum = jnp.einsum(
        "chp,phd->chd", weights.astype(jnp.bfloat16), values, preferred_element_type=jnp.float32
    )
    return (highest, totals, accum)


def write_cache(fresh_rows, cache_block, positions, length, group):
    offset = positions - length
    inside = (offset >= 0) & (offset < group)
    taken = jnp.take(fresh_rows, jnp.clip(offset, 0, group - 1), axis=0)
    return jnp.where(inside[:, None, None], taken, cache_block)


def shards(hidden, ln_gain, w_qkv, w_out, kv_cache, cache_len):
    hidden_f = hidden.astype(jnp.float32)
    sums = gy_sum(jnp.stack([jnp.sum(hidden_f, axis=1), jnp.sum(hidden_f * hidden_f, axis=1)]))
    mean = sums[0] / D
    var = sums[1] / D - mean * mean
    normed = (
        (hidden_f - mean[:, None]) * lax.rsqrt(var + norm_eps)[:, None] * ln_gain[None, :]
    ).astype(jnp.bfloat16)
    local_heads = w_qkv.shape[1]
    head_size = w_qkv.shape[2] // 3
    weight_flat = w_qkv.reshape(w_qkv.shape[0], local_heads * 3 * head_size)
    partial_value = jnp.dot(
        ring_gather(normed, "gx"),
        weight_flat,
        preferred_element_type=jnp.float32,
    )
    requests = cache_len.shape[0]
    all_rows = partial_value.shape[0]
    group = all_rows // requests
    width_local = local_heads * head_size
    block = kv_cache.shape[1]
    positions = gy_index() * block + jnp.arange(block, dtype=jnp.int32)
    head_ids = lax.axis_index("gx") * local_heads + jnp.arange(local_heads, dtype=jnp.int32)
    all_heads = local_heads * lax.axis_size("gx")
    slopes = jnp.exp2(-8.0 * (head_ids + 1).astype(jnp.float32) / all_heads)
    scale = 1.0 / math.sqrt(head_size)
    steps_c = jnp.arange(group, dtype=jnp.int32)
    tops_list = []
    totals_list = []
    accum_list = []
    caches = []
    qkv = gy_sum_rows(partial_value.astype(jnp.bfloat16))
    qkv = qkv.reshape(requests, group, local_heads, 3 * head_size)
    fresh = jnp.stack(
        [
            qkv[:, :, :, head_size : 2 * head_size].reshape(requests, group, width_local),
            qkv[:, :, :, 2 * head_size :].reshape(requests, group, width_local),
        ],
        axis=2,
    )
    for request in range(requests):
        length = cache_len[request]
        updated = write_cache(fresh[request], kv_cache[request], positions, length, group)
        caches.append(updated)
        keys = updated[:, 0].reshape(block, local_heads, head_size)
        values = updated[:, 1].reshape(block, local_heads, head_size)
        distance = (length + steps_c)[:, None] - positions[None, :]
        part_top, part_total, part_accum = partial_attend(
            qkv[request, :, :, :head_size], keys, values, distance >= 0, distance, slopes, scale
        )
        tops_list.append(part_top)
        totals_list.append(part_total)
        accum_list.append(part_accum)
    tops = jnp.stack(tops_list)
    totals = jnp.stack(totals_list)
    accums = jnp.stack(accum_list)
    rows = requests * group
    packed = jnp.concatenate(
        [
            accums.astype(jnp.bfloat16).reshape(rows, width_local),
            totals.astype(jnp.bfloat16).reshape(rows, local_heads),
        ],
        axis=1,
    )
    attn = attend_combine(packed, tops.reshape(rows, local_heads), local_heads)
    projected = ring_scatter_sum(
        jnp.dot(attn, w_out, preferred_element_type=jnp.float32).astype(jnp.bfloat16), "gx"
    )
    mixed = (projected + hidden_f).astype(jnp.bfloat16)
    return (mixed, jnp.stack(caches))


def solution(mesh):
    n_gy = mesh.shape["gy"]
    split = Mesh(
        mesh.devices.reshape(mesh.shape["req"], mesh.shape["gx"], n_gy // 2, 2),
        ("req", "gx") + GY,
    )
    in_specs = (
        P(("req", "gx"), GY),
        P(GY),
        P(GY, "gx", None),
        P("gx", GY),
        P("req", GY, None, "gx"),
        P("req"),
    )
    out_specs = (P(("req", "gx"), GY), P("req", GY, None, "gx"))
    return jax.shard_map(shards, mesh=split, in_specs=in_specs, out_specs=out_specs, check_vma=False)
```

```python
import math

import jax
import jax.numpy as jnp
from jax import lax
from jax.sharding import Mesh
from jax.sharding import PartitionSpec as P

D = 4096


norm_eps = 1e-05
floor_score = -1e30


GY = ("gyy", "gyz")


def gy_index():
    return lax.axis_index("gyy") * lax.axis_size("gyz") + lax.axis_index("gyz")


def shift(x, axis, step):
    n = lax.axis_size(axis)
    return lax.ppermute(x, axis, [(i, (i + step) % n) for i in range(n)])


def swap_combine(x, axis, op):
    wide = x.astype(jnp.float32) if op is jnp.add else x
    total = wide
    for step in range(1, lax.axis_size(axis)):
        total = op(total, shift(x, axis, step).astype(wide.dtype))
    return total


def ring_scatter_sum(x, axis):
    n = lax.axis_size(axis)
    me = lax.axis_index(axis)
    rows = x.shape[0] // n
    total = lax.dynamic_slice_in_dim(x, me * rows, rows).astype(jnp.float32)
    for step in range(1, n):
        block = lax.dynamic_slice_in_dim(x, ((me + step) % n) * rows, rows)
        total = total + shift(block, axis, step).astype(jnp.float32)
    return total


def ring_gather(x, axis):
    n = lax.axis_size(axis)
    me = lax.axis_index(axis)
    stacked = jnp.stack([x] + [shift(x, axis, step) for step in range(1, n)])
    order = (me - jnp.arange(n, dtype=jnp.int32)) % n
    taken = jnp.take(stacked, order, axis=0)
    return taken.reshape((n * x.shape[0],) + x.shape[1:])


def exchange_scatter_sum(x, axis):
    n = lax.axis_size(axis)
    split = x.reshape((n, x.shape[0] // n) + x.shape[1:])
    return jnp.sum(lax.all_to_all(split, axis, 0, 0).astype(jnp.float32), axis=0)


def exchange_gather(x, axis):
    n = lax.axis_size(axis)
    copies = jnp.broadcast_to(x[None], (n,) + x.shape)
    return lax.all_to_all(copies, axis, 0, 0).reshape((n * x.shape[0],) + x.shape[1:])


def split3(x):
    pieces = []
    for _ in range(3):
        piece = x.astype(jnp.bfloat16)
        pieces.append(piece)
        x = x - piece.astype(jnp.float32)
    return jnp.concatenate(pieces, axis=1)


def join3(x, heads):
    wide = x.astype(jnp.float32)
    return wide[:, :heads] + wide[:, heads : 2 * heads] + wide[:, 2 * heads :]


def merge(parts, heads):
    parts = [(block[:, : -3 * heads], join3(block[:, -3 * heads :], heads)) for block in parts]
    top = parts[0][1]
    for _, high in parts[1:]:
        top = jnp.maximum(top, high)
    total = 0.0
    for block, high in parts:
        factor = jnp.exp(high - top)
        wide = jnp.repeat(factor, block.shape[1] // heads - 1, axis=1)
        total = total + block.astype(jnp.float32) * jnp.concatenate([wide, factor], axis=1)
    return total, top


def attend_combine(packed, tops, heads):
    n = lax.axis_size("gyy")
    me = lax.axis_index("gyy")
    rows = packed.shape[0] // n
    packed = jnp.concatenate([packed, split3(tops)], axis=1)
    split = packed.reshape((n, rows) + packed.shape[1:])
    received = lax.all_to_all(split, "gyy", 0, 0)
    total, top = merge([received[j] for j in range(n)], heads)
    own = jnp.concatenate([total.astype(packed.dtype), split3(top)], axis=1)
    total, _ = merge([own, shift(own, "gyz", 1)], heads)
    width = total.shape[1] - heads
    sums = total[:, :width].reshape(rows, heads, width // heads)
    attn = (sums / total[:, width:, None]).astype(packed.dtype).reshape(rows, width)
    return exchange_gather(attn, "gyy")


def gy_sum(x):
    n = lax.axis_size("gyy") * lax.axis_size("gyz")
    copies = jnp.broadcast_to(x[None], (n,) + x.shape)
    return jnp.sum(lax.all_to_all(copies, GY, 0, 0), axis=0)


def gy_max(x):
    return swap_combine(swap_combine(x, "gyz", jnp.maximum), "gyy", jnp.maximum)


def gy_sum_rows(x):
    part = exchange_scatter_sum(x, "gyy").astype(x.dtype)
    part = swap_combine(part, "gyz", jnp.add).astype(x.dtype)
    return exchange_gather(part, "gyy")


def partial_attend(query, keys, values, valid, distance, slopes, scale):
    scores = jnp.einsum("chd,phd->chp", query, keys, preferred_element_type=jnp.float32) * scale
    scores = scores - slopes[None, :, None] * distance.astype(jnp.float32)[:, None, :]
    scores = jnp.where(valid[:, None, :], scores, floor_score)
    highest = jnp.max(scores, axis=-1)
    weights = jnp.where(valid[:, None, :], jnp.exp(scores - highest[..., None]), 0.0)
    totals = jnp.sum(weights, axis=-1)
    accum = jnp.einsum(
        "chp,phd->chd", weights.astype(jnp.bfloat16), values, preferred_element_type=jnp.float32
    )
    return (highest, totals, accum)


def write_cache(fresh_rows, cache_block, positions, length, group):
    offset = positions - length
    inside = (offset >= 0) & (offset < group)
    taken = jnp.take(fresh_rows, jnp.clip(offset, 0, group - 1), axis=0)
    return jnp.where(inside[:, None, None], taken, cache_block)


def shards(hidden, ln_gain, w_qkv, w_out, kv_cache, cache_len):
    hidden_f = hidden.astype(jnp.float32)
    sums = gy_sum(jnp.stack([jnp.sum(hidden_f, axis=1), jnp.sum(hidden_f * hidden_f, axis=1)]))
    mean = sums[0] / D
    var = sums[1] / D - mean * mean
    normed = (
        (hidden_f - mean[:, None]) * lax.rsqrt(var + norm_eps)[:, None] * ln_gain[None, :]
    ).astype(jnp.bfloat16)
    local_heads = w_qkv.shape[1]
    head_size = w_qkv.shape[2] // 3
    weight_flat = w_qkv.reshape(w_qkv.shape[0], local_heads * 3 * head_size)
    partial_value = jnp.dot(
        exchange_gather(normed, "gx"),
        weight_flat,
        preferred_element_type=jnp.float32,
    )
    requests = cache_len.shape[0]
    all_rows = partial_value.shape[0]
    group = all_rows // requests
    width_local = local_heads * head_size
    block = kv_cache.shape[1]
    positions = gy_index() * block + jnp.arange(block, dtype=jnp.int32)
    head_ids = lax.axis_index("gx") * local_heads + jnp.arange(local_heads, dtype=jnp.int32)
    all_heads = local_heads * lax.axis_size("gx")
    slopes = jnp.exp2(-8.0 * (head_ids + 1).astype(jnp.float32) / all_heads)
    scale = 1.0 / math.sqrt(head_size)
    steps_c = jnp.arange(group, dtype=jnp.int32)
    tops_list = []
    totals_list = []
    accum_list = []
    caches = []
    qkv = gy_sum_rows(partial_value.astype(jnp.bfloat16))
    qkv = qkv.reshape(requests, group, local_heads, 3 * head_size)
    fresh = jnp.stack(
        [
            qkv[:, :, :, head_size : 2 * head_size].reshape(requests, group, width_local),
            qkv[:, :, :, 2 * head_size :].reshape(requests, group, width_local),
        ],
        axis=2,
    )
    for request in range(requests):
        length = cache_len[request]
        updated = write_cache(fresh[request], kv_cache[request], positions, length, group)
        caches.append(updated)
        keys = updated[:, 0].reshape(block, local_heads, head_size)
        values = updated[:, 1].reshape(block, local_heads, head_size)
        distance = (length + steps_c)[:, None] - positions[None, :]
        part_top, part_total, part_accum = partial_attend(
            qkv[request, :, :, :head_size], keys, values, distance >= 0, distance, slopes, scale
        )
        tops_list.append(part_top)
        totals_list.append(part_total)
        accum_list.append(part_accum)
    tops = jnp.stack(tops_list)
    totals = jnp.stack(totals_list)
    accums = jnp.stack(accum_list)
    rows = requests * group
    packed = jnp.concatenate(
        [
            accums.astype(jnp.bfloat16).reshape(rows, width_local),
            totals.astype(jnp.bfloat16).reshape(rows, local_heads),
        ],
        axis=1,
    )
    attn = attend_combine(packed, tops.reshape(rows, local_heads), local_heads)
    projected = exchange_scatter_sum(
        jnp.dot(attn, w_out, preferred_element_type=jnp.float32).astype(jnp.bfloat16), "gx"
    )
    mixed = (projected + hidden_f).astype(jnp.bfloat16)
    return (mixed, jnp.stack(caches))


def solution(mesh):
    n_gy = mesh.shape["gy"]
    split = Mesh(
        mesh.devices.reshape(mesh.shape["req"], mesh.shape["gx"], n_gy // 2, 2),
        ("req", "gx") + GY,
    )
    in_specs = (
        P(("req", "gx"), GY),
        P(GY),
        P(GY, "gx", None),
        P("gx", GY),
        P("req", GY, None, "gx"),
        P("req"),
    )
    out_specs = (P(("req", "gx"), GY), P("req", GY, None, "gx"))
    return jax.shard_map(shards, mesh=split, in_specs=in_specs, out_specs=out_specs, check_vma=False)
```

```python
import math

import jax
import jax.numpy as jnp
from jax import lax
from jax.sharding import Mesh
from jax.sharding import PartitionSpec as P

D = 4096


norm_eps = 1e-05
floor_score = -1e30


GY = ("gyy", "gyz")


def gy_index():
    return lax.axis_index("gyy") * lax.axis_size("gyz") + lax.axis_index("gyz")


def shift(x, axis, step):
    n = lax.axis_size(axis)
    return lax.ppermute(x, axis, [(i, (i + step) % n) for i in range(n)])


def swap_combine(x, axis, op):
    wide = x.astype(jnp.float32) if op is jnp.add else x
    total = wide
    for step in range(1, lax.axis_size(axis)):
        total = op(total, shift(x, axis, step).astype(wide.dtype))
    return total


def ring_scatter_sum(x, axis):
    n = lax.axis_size(axis)
    me = lax.axis_index(axis)
    rows = x.shape[0] // n
    total = lax.dynamic_slice_in_dim(x, me * rows, rows).astype(jnp.float32)
    for step in range(1, n):
        block = lax.dynamic_slice_in_dim(x, ((me + step) % n) * rows, rows)
        total = total + shift(block, axis, step).astype(jnp.float32)
    return total


def ring_gather(x, axis):
    n = lax.axis_size(axis)
    me = lax.axis_index(axis)
    stacked = jnp.stack([x] + [shift(x, axis, step) for step in range(1, n)])
    order = (me - jnp.arange(n, dtype=jnp.int32)) % n
    taken = jnp.take(stacked, order, axis=0)
    return taken.reshape((n * x.shape[0],) + x.shape[1:])


def exchange_scatter_sum(x, axis):
    n = lax.axis_size(axis)
    split = x.reshape((n, x.shape[0] // n) + x.shape[1:])
    return jnp.sum(lax.all_to_all(split, axis, 0, 0).astype(jnp.float32), axis=0)


def exchange_gather(x, axis):
    n = lax.axis_size(axis)
    copies = jnp.broadcast_to(x[None], (n,) + x.shape)
    return lax.all_to_all(copies, axis, 0, 0).reshape((n * x.shape[0],) + x.shape[1:])


def split3(x):
    pieces = []
    for _ in range(3):
        piece = x.astype(jnp.bfloat16)
        pieces.append(piece)
        x = x - piece.astype(jnp.float32)
    return jnp.concatenate(pieces, axis=1)


def join3(x, heads):
    wide = x.astype(jnp.float32)
    return wide[:, :heads] + wide[:, heads : 2 * heads] + wide[:, 2 * heads :]


def merge(parts, heads):
    parts = [(block[:, : -3 * heads], join3(block[:, -3 * heads :], heads)) for block in parts]
    top = parts[0][1]
    for _, high in parts[1:]:
        top = jnp.maximum(top, high)
    total = 0.0
    for block, high in parts:
        factor = jnp.exp(high - top)
        wide = jnp.repeat(factor, block.shape[1] // heads - 1, axis=1)
        total = total + block.astype(jnp.float32) * jnp.concatenate([wide, factor], axis=1)
    return total, top


def attend_combine(packed, tops, heads):
    n = lax.axis_size("gyy")
    me = lax.axis_index("gyy")
    rows = packed.shape[0] // n
    packed = jnp.concatenate([packed, split3(tops)], axis=1)
    split = packed.reshape((n, rows) + packed.shape[1:])
    received = lax.all_to_all(split, "gyy", 0, 0)
    total, top = merge([received[j] for j in range(n)], heads)
    own = jnp.concatenate([total.astype(packed.dtype), split3(top)], axis=1)
    total, _ = merge([own, shift(own, "gyz", 1)], heads)
    width = total.shape[1] - heads
    sums = total[:, :width].reshape(rows, heads, width // heads)
    attn = (sums / total[:, width:, None]).astype(packed.dtype).reshape(rows, width)
    return exchange_gather(attn, "gyy")


def gy_sum(x):
    n = lax.axis_size("gyy") * lax.axis_size("gyz")
    copies = jnp.broadcast_to(x[None], (n,) + x.shape)
    return jnp.sum(lax.all_to_all(copies, GY, 0, 0), axis=0)


def gy_max(x):
    return swap_combine(swap_combine(x, "gyz", jnp.maximum), "gyy", jnp.maximum)


def gy_sum_rows(x):
    part = exchange_scatter_sum(x, "gyy").astype(x.dtype)
    part = swap_combine(part, "gyz", jnp.add).astype(x.dtype)
    return exchange_gather(part, "gyy")


def partial_attend(query, keys, values, valid, distance, slopes, scale):
    scores = jnp.einsum("chd,phd->chp", query, keys, preferred_element_type=jnp.float32) * scale
    scores = scores - slopes[None, :, None] * distance.astype(jnp.float32)[:, None, :]
    scores = jnp.where(valid[:, None, :], scores, floor_score)
    highest = jnp.max(scores, axis=-1)
    weights = jnp.where(valid[:, None, :], jnp.exp(scores - highest[..., None]), 0.0)
    totals = jnp.sum(weights, axis=-1)
    accum = jnp.einsum(
        "chp,phd->chd", weights.astype(jnp.bfloat16), values, preferred_element_type=jnp.float32
    )
    return (highest, totals, accum)


def write_cache(fresh_rows, cache_block, positions, length, group):
    offset = positions - length
    inside = (offset >= 0) & (offset < group)
    taken = jnp.take(fresh_rows, jnp.clip(offset, 0, group - 1), axis=0)
    return jnp.where(inside[:, None, None], taken, cache_block)


def shards(hidden, ln_gain, w_qkv, w_out, kv_cache, cache_len):
    hidden_f = hidden.astype(jnp.float32)
    sums = gy_sum(jnp.stack([jnp.sum(hidden_f, axis=1), jnp.sum(hidden_f * hidden_f, axis=1)]))
    mean = sums[0] / D
    var = sums[1] / D - mean * mean
    normed = (
        (hidden_f - mean[:, None]) * lax.rsqrt(var + norm_eps)[:, None] * ln_gain[None, :]
    ).astype(jnp.bfloat16)
    local_heads = w_qkv.shape[1]
    head_size = w_qkv.shape[2] // 3
    weight_flat = w_qkv.reshape(w_qkv.shape[0], local_heads * 3 * head_size)
    partial_value = jnp.dot(
        ring_gather(normed, "gx"),
        weight_flat,
        preferred_element_type=jnp.float32,
    )
    requests = cache_len.shape[0]
    all_rows = partial_value.shape[0]
    group = all_rows // requests
    width_local = local_heads * head_size
    block = kv_cache.shape[1]
    positions = gy_index() * block + jnp.arange(block, dtype=jnp.int32)
    head_ids = lax.axis_index("gx") * local_heads + jnp.arange(local_heads, dtype=jnp.int32)
    all_heads = local_heads * lax.axis_size("gx")
    slopes = jnp.exp2(-8.0 * (head_ids + 1).astype(jnp.float32) / all_heads)
    scale = 1.0 / math.sqrt(head_size)
    steps_c = jnp.arange(group, dtype=jnp.int32)
    tops_list = []
    totals_list = []
    accum_list = []
    caches = []
    qkv = gy_sum_rows(partial_value.astype(jnp.bfloat16))
    qkv = qkv.reshape(requests, group, local_heads, 3 * head_size)
    fresh = jnp.stack(
        [
            qkv[:, :, :, head_size : 2 * head_size].reshape(requests, group, width_local),
            qkv[:, :, :, 2 * head_size :].reshape(requests, group, width_local),
        ],
        axis=2,
    )
    for request in range(requests):
        length = cache_len[request]
        updated = write_cache(fresh[request], kv_cache[request], positions, length, group)
        caches.append(updated)
        keys = updated[:, 0].reshape(block, local_heads, head_size)
        values = updated[:, 1].reshape(block, local_heads, head_size)
        distance = (length + steps_c)[:, None] - positions[None, :]
        part_top, part_total, part_accum = partial_attend(
            qkv[request, :, :, :head_size], keys, values, distance >= 0, distance, slopes, scale
        )
        tops_list.append(part_top)
        totals_list.append(part_total)
        accum_list.append(part_accum)
    tops = jnp.stack(tops_list)
    totals = jnp.stack(totals_list)
    accums = jnp.stack(accum_list)
    rows = requests * group
    packed = jnp.concatenate(
        [
            accums.astype(jnp.bfloat16).reshape(rows, width_local),
            totals.astype(jnp.bfloat16).reshape(rows, local_heads),
        ],
        axis=1,
    )
    attn = attend_combine(packed, tops.reshape(rows, local_heads), local_heads)
    projected = ring_scatter_sum(
        jnp.dot(attn, w_out, preferred_element_type=jnp.float32).astype(jnp.bfloat16), "gx"
    )
    mixed = (projected + hidden_f).astype(jnp.bfloat16)
    return (mixed, jnp.stack(caches))


def solution(mesh):
    n_gy = mesh.shape["gy"]
    split = Mesh(
        mesh.devices.reshape(mesh.shape["req"], mesh.shape["gx"], n_gy // 2, 2),
        ("req", "gx") + GY,
    )
    in_specs = (
        P(("req", "gx"), GY),
        P(GY),
        P(GY, "gx", None),
        P("gx", GY),
        P("req", GY, None, "gx"),
        P("req"),
    )
    out_specs = (P(("req", "gx"), GY), P("req", GY, None, "gx"))
    return jax.shard_map(shards, mesh=split, in_specs=in_specs, out_specs=out_specs, check_vma=False)
```

```python
import math

import jax
import jax.numpy as jnp
from jax import lax
from jax.sharding import Mesh
from jax.sharding import PartitionSpec as P

D = 4096


norm_eps = 1e-05
floor_score = -1e30


GY = ("gyy", "gyz")


def gy_index():
    return lax.axis_index("gyy") * lax.axis_size("gyz") + lax.axis_index("gyz")


def shift(x, axis, step):
    n = lax.axis_size(axis)
    return lax.ppermute(x, axis, [(i, (i + step) % n) for i in range(n)])


def swap_combine(x, axis, op):
    wide = x.astype(jnp.float32) if op is jnp.add else x
    total = wide
    for step in range(1, lax.axis_size(axis)):
        total = op(total, shift(x, axis, step).astype(wide.dtype))
    return total


def ring_scatter_sum(x, axis):
    n = lax.axis_size(axis)
    me = lax.axis_index(axis)
    rows = x.shape[0] // n
    total = lax.dynamic_slice_in_dim(x, me * rows, rows).astype(jnp.float32)
    for step in range(1, n):
        block = lax.dynamic_slice_in_dim(x, ((me + step) % n) * rows, rows)
        total = total + shift(block, axis, step).astype(jnp.float32)
    return total


def ring_gather(x, axis):
    n = lax.axis_size(axis)
    me = lax.axis_index(axis)
    stacked = jnp.stack([x] + [shift(x, axis, step) for step in range(1, n)])
    order = (me - jnp.arange(n, dtype=jnp.int32)) % n
    taken = jnp.take(stacked, order, axis=0)
    return taken.reshape((n * x.shape[0],) + x.shape[1:])


def exchange_scatter_sum(x, axis):
    n = lax.axis_size(axis)
    split = x.reshape((n, x.shape[0] // n) + x.shape[1:])
    return jnp.sum(lax.all_to_all(split, axis, 0, 0).astype(jnp.float32), axis=0)


def exchange_gather(x, axis):
    n = lax.axis_size(axis)
    copies = jnp.broadcast_to(x[None], (n,) + x.shape)
    return lax.all_to_all(copies, axis, 0, 0).reshape((n * x.shape[0],) + x.shape[1:])


def split3(x):
    pieces = []
    for _ in range(3):
        piece = x.astype(jnp.bfloat16)
        pieces.append(piece)
        x = x - piece.astype(jnp.float32)
    return jnp.concatenate(pieces, axis=1)


def join3(x, heads):
    wide = x.astype(jnp.float32)
    return wide[:, :heads] + wide[:, heads : 2 * heads] + wide[:, 2 * heads :]


def merge(parts, heads):
    parts = [(block[:, : -3 * heads], join3(block[:, -3 * heads :], heads)) for block in parts]
    top = parts[0][1]
    for _, high in parts[1:]:
        top = jnp.maximum(top, high)
    total = 0.0
    for block, high in parts:
        factor = jnp.exp(high - top)
        wide = jnp.repeat(factor, block.shape[1] // heads - 1, axis=1)
        total = total + block.astype(jnp.float32) * jnp.concatenate([wide, factor], axis=1)
    return total, top


def attend_combine(packed, tops, heads):
    n = lax.axis_size("gyy")
    me = lax.axis_index("gyy")
    rows = packed.shape[0] // n
    packed = jnp.concatenate([packed, split3(tops)], axis=1)
    split = packed.reshape((n, rows) + packed.shape[1:])
    received = lax.all_to_all(split, "gyy", 0, 0)
    total, top = merge([received[j] for j in range(n)], heads)
    own = jnp.concatenate([total.astype(packed.dtype), split3(top)], axis=1)
    total, _ = merge([own, shift(own, "gyz", 1)], heads)
    width = total.shape[1] - heads
    sums = total[:, :width].reshape(rows, heads, width // heads)
    attn = (sums / total[:, width:, None]).astype(packed.dtype).reshape(rows, width)
    return exchange_gather(attn, "gyy")


def gy_sum(x):
    n = lax.axis_size("gyy") * lax.axis_size("gyz")
    copies = jnp.broadcast_to(x[None], (n,) + x.shape)
    return jnp.sum(lax.all_to_all(copies, GY, 0, 0), axis=0)


def gy_max(x):
    return swap_combine(swap_combine(x, "gyz", jnp.maximum), "gyy", jnp.maximum)


def gy_sum_rows(x):
    part = exchange_scatter_sum(x, "gyy").astype(x.dtype)
    part = swap_combine(part, "gyz", jnp.add).astype(x.dtype)
    return exchange_gather(part, "gyy")


def partial_attend(query, keys, values, valid, distance, slopes, scale):
    scores = jnp.einsum("chd,phd->chp", query, keys, preferred_element_type=jnp.float32) * scale
    scores = scores - slopes[None, :, None] * distance.astype(jnp.float32)[:, None, :]
    scores = jnp.where(valid[:, None, :], scores, floor_score)
    highest = jnp.max(scores, axis=-1)
    weights = jnp.where(valid[:, None, :], jnp.exp(scores - highest[..., None]), 0.0)
    totals = jnp.sum(weights, axis=-1)
    accum = jnp.einsum(
        "chp,phd->chd", weights.astype(jnp.bfloat16), values, preferred_element_type=jnp.float32
    )
    return (highest, totals, accum)


def write_cache(fresh_rows, cache_block, positions, length, group):
    offset = positions - length
    inside = (offset >= 0) & (offset < group)
    taken = jnp.take(fresh_rows, jnp.clip(offset, 0, group - 1), axis=0)
    return jnp.where(inside[:, None, None], taken, cache_block)


def shards(hidden, ln_gain, w_qkv, w_out, kv_cache, cache_len):
    hidden_f = hidden.astype(jnp.float32)
    gathered = ring_gather(hidden, "gx").astype(jnp.float32)
    sums = gy_sum(jnp.stack([jnp.sum(hidden_f, axis=1), jnp.sum(hidden_f * hidden_f, axis=1)], axis=1))
    sums = exchange_gather(sums, "gx")
    mean = sums[:, 0] / D
    var = sums[:, 1] / D - mean * mean
    normed = (
        (gathered - mean[:, None]) * lax.rsqrt(var + norm_eps)[:, None] * ln_gain[None, :]
    ).astype(jnp.bfloat16)
    local_heads = w_qkv.shape[1]
    head_size = w_qkv.shape[2] // 3
    weight_flat = w_qkv.reshape(w_qkv.shape[0], local_heads * 3 * head_size)
    partial_value = jnp.dot(
        normed,
        weight_flat,
        preferred_element_type=jnp.float32,
    )
    requests = cache_len.shape[0]
    all_rows = partial_value.shape[0]
    group = all_rows // requests
    width_local = local_heads * head_size
    block = kv_cache.shape[1]
    positions = gy_index() * block + jnp.arange(block, dtype=jnp.int32)
    head_ids = lax.axis_index("gx") * local_heads + jnp.arange(local_heads, dtype=jnp.int32)
    all_heads = local_heads * lax.axis_size("gx")
    slopes = jnp.exp2(-8.0 * (head_ids + 1).astype(jnp.float32) / all_heads)
    scale = 1.0 / math.sqrt(head_size)
    steps_c = jnp.arange(group, dtype=jnp.int32)
    tops_list = []
    totals_list = []
    accum_list = []
    caches = []
    qkv = gy_sum_rows(partial_value.astype(jnp.bfloat16))
    qkv = qkv.reshape(requests, group, local_heads, 3 * head_size)
    fresh = jnp.stack(
        [
            qkv[:, :, :, head_size : 2 * head_size].reshape(requests, group, width_local),
            qkv[:, :, :, 2 * head_size :].reshape(requests, group, width_local),
        ],
        axis=2,
    )
    for request in range(requests):
        length = cache_len[request]
        updated = write_cache(fresh[request], kv_cache[request], positions, length, group)
        caches.append(updated)
        keys = updated[:, 0].reshape(block, local_heads, head_size)
        values = updated[:, 1].reshape(block, local_heads, head_size)
        distance = (length + steps_c)[:, None] - positions[None, :]
        part_top, part_total, part_accum = partial_attend(
            qkv[request, :, :, :head_size], keys, values, distance >= 0, distance, slopes, scale
        )
        tops_list.append(part_top)
        totals_list.append(part_total)
        accum_list.append(part_accum)
    tops = jnp.stack(tops_list)
    totals = jnp.stack(totals_list)
    accums = jnp.stack(accum_list)
    rows = requests * group
    packed = jnp.concatenate(
        [
            accums.astype(jnp.bfloat16).reshape(rows, width_local),
            totals.astype(jnp.bfloat16).reshape(rows, local_heads),
        ],
        axis=1,
    )
    attn = attend_combine(packed, tops.reshape(rows, local_heads), local_heads)
    projected = ring_scatter_sum(
        jnp.dot(attn, w_out, preferred_element_type=jnp.float32).astype(jnp.bfloat16), "gx"
    )
    mixed = (projected + hidden_f).astype(jnp.bfloat16)
    return (mixed, jnp.stack(caches))


def solution(mesh):
    n_gy = mesh.shape["gy"]
    split = Mesh(
        mesh.devices.reshape(mesh.shape["req"], mesh.shape["gx"], n_gy // 2, 2),
        ("req", "gx") + GY,
    )
    in_specs = (
        P(("req", "gx"), GY),
        P(GY),
        P(GY, "gx", None),
        P("gx", GY),
        P("req", GY, None, "gx"),
        P("req"),
    )
    out_specs = (P(("req", "gx"), GY), P("req", GY, None, "gx"))
    return jax.shard_map(shards, mesh=split, in_specs=in_specs, out_specs=out_specs, check_vma=False)
```

```python
import math

import jax
import jax.numpy as jnp
from jax import lax
from jax.sharding import Mesh
from jax.sharding import PartitionSpec as P

D = 4096


norm_eps = 1e-05
floor_score = -1e30


GY = ("gyy", "gyz")


def gy_index():
    return lax.axis_index("gyy") * lax.axis_size("gyz") + lax.axis_index("gyz")


def shift(x, axis, step):
    n = lax.axis_size(axis)
    return lax.ppermute(x, axis, [(i, (i + step) % n) for i in range(n)])


def swap_combine(x, axis, op):
    wide = x.astype(jnp.float32) if op is jnp.add else x
    total = wide
    for step in range(1, lax.axis_size(axis)):
        total = op(total, shift(x, axis, step).astype(wide.dtype))
    return total


def ring_scatter_sum(x, axis):
    n = lax.axis_size(axis)
    me = lax.axis_index(axis)
    rows = x.shape[0] // n
    total = lax.dynamic_slice_in_dim(x, me * rows, rows).astype(jnp.float32)
    for step in range(1, n):
        block = lax.dynamic_slice_in_dim(x, ((me + step) % n) * rows, rows)
        total = total + shift(block, axis, step).astype(jnp.float32)
    return total


def ring_gather(x, axis):
    n = lax.axis_size(axis)
    me = lax.axis_index(axis)
    stacked = jnp.stack([x] + [shift(x, axis, step) for step in range(1, n)])
    order = (me - jnp.arange(n, dtype=jnp.int32)) % n
    taken = jnp.take(stacked, order, axis=0)
    return taken.reshape((n * x.shape[0],) + x.shape[1:])


def exchange_scatter_sum(x, axis):
    n = lax.axis_size(axis)
    split = x.reshape((n, x.shape[0] // n) + x.shape[1:])
    return jnp.sum(lax.all_to_all(split, axis, 0, 0).astype(jnp.float32), axis=0)


def exchange_gather(x, axis):
    n = lax.axis_size(axis)
    copies = jnp.broadcast_to(x[None], (n,) + x.shape)
    return lax.all_to_all(copies, axis, 0, 0).reshape((n * x.shape[0],) + x.shape[1:])


def split3(x):
    pieces = []
    for _ in range(3):
        piece = x.astype(jnp.bfloat16)
        pieces.append(piece)
        x = x - piece.astype(jnp.float32)
    return jnp.concatenate(pieces, axis=1)


def join3(x, heads):
    wide = x.astype(jnp.float32)
    return wide[:, :heads] + wide[:, heads : 2 * heads] + wide[:, 2 * heads :]


def merge(parts, heads):
    parts = [(block[:, : -3 * heads], join3(block[:, -3 * heads :], heads)) for block in parts]
    top = parts[0][1]
    for _, high in parts[1:]:
        top = jnp.maximum(top, high)
    total = 0.0
    for block, high in parts:
        factor = jnp.exp(high - top)
        wide = jnp.repeat(factor, block.shape[1] // heads - 1, axis=1)
        total = total + block.astype(jnp.float32) * jnp.concatenate([wide, factor], axis=1)
    return total, top


def attend_combine(packed, tops, heads):
    n = lax.axis_size("gyy")
    me = lax.axis_index("gyy")
    rows = packed.shape[0] // n
    packed = jnp.concatenate([packed, split3(tops)], axis=1)
    split = packed.reshape((n, rows) + packed.shape[1:])
    received = lax.all_to_all(split, "gyy", 0, 0)
    total, top = merge([received[j] for j in range(n)], heads)
    own = jnp.concatenate([total.astype(packed.dtype), split3(top)], axis=1)
    total, _ = merge([own, shift(own, "gyz", 1)], heads)
    width = total.shape[1] - heads
    sums = total[:, :width].reshape(rows, heads, width // heads)
    attn = (sums / total[:, width:, None]).astype(packed.dtype).reshape(rows, width)
    return exchange_gather(attn, "gyy")


def gy_sum(x):
    n = lax.axis_size("gyy") * lax.axis_size("gyz")
    copies = jnp.broadcast_to(x[None], (n,) + x.shape)
    return jnp.sum(lax.all_to_all(copies, GY, 0, 0), axis=0)


def gy_max(x):
    return swap_combine(swap_combine(x, "gyz", jnp.maximum), "gyy", jnp.maximum)


def gy_sum_rows(x):
    part = exchange_scatter_sum(x, "gyy").astype(x.dtype)
    part = swap_combine(part, "gyz", jnp.add).astype(x.dtype)
    return exchange_gather(part, "gyy")


def partial_attend(query, keys, values, valid, distance, slopes, scale):
    scores = jnp.einsum("chd,phd->chp", query, keys, preferred_element_type=jnp.float32) * scale
    scores = scores - slopes[None, :, None] * distance.astype(jnp.float32)[:, None, :]
    scores = jnp.where(valid[:, None, :], scores, floor_score)
    highest = jnp.max(scores, axis=-1)
    weights = jnp.where(valid[:, None, :], jnp.exp(scores - highest[..., None]), 0.0)
    totals = jnp.sum(weights, axis=-1)
    accum = jnp.einsum(
        "chp,phd->chd", weights.astype(jnp.bfloat16), values, preferred_element_type=jnp.float32
    )
    return (highest, totals, accum)


def write_cache(fresh_rows, cache_block, positions, length, group):
    offset = positions - length
    inside = (offset >= 0) & (offset < group)
    block = cache_block.shape[0]
    padded = jnp.pad(fresh_rows, ((block, block), (0, 0), (0, 0)))
    start = jnp.clip(offset[0] + block, 0, group + block)
    taken = lax.dynamic_slice_in_dim(padded, start, block, axis=0)
    return jnp.where(inside[:, None, None], taken, cache_block)


def shards(hidden, ln_gain, w_qkv, w_out, kv_cache, cache_len):
    hidden_f = hidden.astype(jnp.float32)
    sums = gy_sum(jnp.stack([jnp.sum(hidden_f, axis=1), jnp.sum(hidden_f * hidden_f, axis=1)]))
    mean = sums[0] / D
    var = sums[1] / D - mean * mean
    normed = (
        (hidden_f - mean[:, None]) * lax.rsqrt(var + norm_eps)[:, None] * ln_gain[None, :]
    ).astype(jnp.bfloat16)
    local_heads = w_qkv.shape[1]
    head_size = w_qkv.shape[2] // 3
    weight_flat = w_qkv.reshape(w_qkv.shape[0], local_heads * 3 * head_size)
    partial_value = jnp.dot(
        ring_gather(normed, "gx"),
        weight_flat,
        preferred_element_type=jnp.float32,
    )
    requests = cache_len.shape[0]
    all_rows = partial_value.shape[0]
    group = all_rows // requests
    width_local = local_heads * head_size
    block = kv_cache.shape[1]
    positions = gy_index() * block + jnp.arange(block, dtype=jnp.int32)
    head_ids = lax.axis_index("gx") * local_heads + jnp.arange(local_heads, dtype=jnp.int32)
    all_heads = local_heads * lax.axis_size("gx")
    slopes = jnp.exp2(-8.0 * (head_ids + 1).astype(jnp.float32) / all_heads)
    scale = 1.0 / math.sqrt(head_size)
    steps_c = jnp.arange(group, dtype=jnp.int32)
    tops_list = []
    totals_list = []
    accum_list = []
    caches = []
    qkv = gy_sum_rows(partial_value.astype(jnp.bfloat16))
    qkv = qkv.reshape(requests, group, local_heads, 3 * head_size)
    fresh = jnp.stack(
        [
            qkv[:, :, :, head_size : 2 * head_size].reshape(requests, group, width_local),
            qkv[:, :, :, 2 * head_size :].reshape(requests, group, width_local),
        ],
        axis=2,
    )
    for request in range(requests):
        length = cache_len[request]
        updated = write_cache(fresh[request], kv_cache[request], positions, length, group)
        caches.append(updated)
        keys = updated[:, 0].reshape(block, local_heads, head_size)
        values = updated[:, 1].reshape(block, local_heads, head_size)
        distance = (length + steps_c)[:, None] - positions[None, :]
        part_top, part_total, part_accum = partial_attend(
            qkv[request, :, :, :head_size], keys, values, distance >= 0, distance, slopes, scale
        )
        tops_list.append(part_top)
        totals_list.append(part_total)
        accum_list.append(part_accum)
    tops = jnp.stack(tops_list)
    totals = jnp.stack(totals_list)
    accums = jnp.stack(accum_list)
    rows = requests * group
    packed = jnp.concatenate(
        [
            accums.astype(jnp.bfloat16).reshape(rows, width_local),
            totals.astype(jnp.bfloat16).reshape(rows, local_heads),
        ],
        axis=1,
    )
    attn = attend_combine(packed, tops.reshape(rows, local_heads), local_heads)
    projected = ring_scatter_sum(
        jnp.dot(attn, w_out, preferred_element_type=jnp.float32).astype(jnp.bfloat16), "gx"
    )
    mixed = (projected + hidden_f).astype(jnp.bfloat16)
    return (mixed, jnp.stack(caches))


def solution(mesh):
    n_gy = mesh.shape["gy"]
    split = Mesh(
        mesh.devices.reshape(mesh.shape["req"], mesh.shape["gx"], n_gy // 2, 2),
        ("req", "gx") + GY,
    )
    in_specs = (
        P(("req", "gx"), GY),
        P(GY),
        P(GY, "gx", None),
        P("gx", GY),
        P("req", GY, None, "gx"),
        P("req"),
    )
    out_specs = (P(("req", "gx"), GY), P("req", GY, None, "gx"))
    return jax.shard_map(shards, mesh=split, in_specs=in_specs, out_specs=out_specs, check_vma=False)
```

```python
import math

import jax
import jax.numpy as jnp
from jax import lax
from jax.sharding import Mesh
from jax.sharding import PartitionSpec as P

D = 4096


norm_eps = 1e-05
floor_score = -1e30


GY = ("gyy", "gyz")


def gy_index():
    return lax.axis_index("gyy") * lax.axis_size("gyz") + lax.axis_index("gyz")


def shift(x, axis, step):
    n = lax.axis_size(axis)
    return lax.ppermute(x, axis, [(i, (i + step) % n) for i in range(n)])


def swap_combine(x, axis, op):
    wide = x.astype(jnp.float32) if op is jnp.add else x
    total = wide
    for step in range(1, lax.axis_size(axis)):
        total = op(total, shift(x, axis, step).astype(wide.dtype))
    return total


def ring_scatter_sum(x, axis):
    n = lax.axis_size(axis)
    me = lax.axis_index(axis)
    rows = x.shape[0] // n
    total = lax.dynamic_slice_in_dim(x, me * rows, rows).astype(jnp.float32)
    for step in range(1, n):
        block = lax.dynamic_slice_in_dim(x, ((me + step) % n) * rows, rows)
        total = total + shift(block, axis, step).astype(jnp.float32)
    return total


def ring_gather(x, axis):
    n = lax.axis_size(axis)
    me = lax.axis_index(axis)
    received = [x] + [shift(x, axis, step) for step in range(1, n)]
    doubled = jnp.stack(received[::-1] * 2)
    taken = lax.dynamic_slice_in_dim(doubled, n - 1 - me, n, axis=0)
    return taken.reshape((n * x.shape[0],) + x.shape[1:])


def exchange_scatter_sum(x, axis):
    n = lax.axis_size(axis)
    split = x.reshape((n, x.shape[0] // n) + x.shape[1:])
    return jnp.sum(lax.all_to_all(split, axis, 0, 0).astype(jnp.float32), axis=0)


def exchange_gather(x, axis):
    n = lax.axis_size(axis)
    copies = jnp.broadcast_to(x[None], (n,) + x.shape)
    return lax.all_to_all(copies, axis, 0, 0).reshape((n * x.shape[0],) + x.shape[1:])


def split3(x):
    pieces = []
    for _ in range(3):
        piece = x.astype(jnp.bfloat16)
        pieces.append(piece)
        x = x - piece.astype(jnp.float32)
    return jnp.concatenate(pieces, axis=1)


def join3(x, heads):
    wide = x.astype(jnp.float32)
    return wide[:, :heads] + wide[:, heads : 2 * heads] + wide[:, 2 * heads :]


def merge(parts, heads):
    parts = [(block[:, : -3 * heads], join3(block[:, -3 * heads :], heads)) for block in parts]
    top = parts[0][1]
    for _, high in parts[1:]:
        top = jnp.maximum(top, high)
    total = 0.0
    for block, high in parts:
        factor = jnp.exp(high - top)
        wide = jnp.repeat(factor, block.shape[1] // heads - 1, axis=1)
        total = total + block.astype(jnp.float32) * jnp.concatenate([wide, factor], axis=1)
    return total, top


def attend_combine(packed, tops, heads):
    n = lax.axis_size("gyy")
    me = lax.axis_index("gyy")
    rows = packed.shape[0] // n
    packed = jnp.concatenate([packed, split3(tops)], axis=1)
    split = packed.reshape((n, rows) + packed.shape[1:])
    received = lax.all_to_all(split, "gyy", 0, 0)
    total, top = merge([received[j] for j in range(n)], heads)
    own = jnp.concatenate([total.astype(packed.dtype), split3(top)], axis=1)
    total, _ = merge([own, shift(own, "gyz", 1)], heads)
    width = total.shape[1] - heads
    sums = total[:, :width].reshape(rows, heads, width // heads)
    attn = (sums / total[:, width:, None]).astype(packed.dtype).reshape(rows, width)
    return exchange_gather(attn, "gyy")


def gy_sum(x):
    n = lax.axis_size("gyy") * lax.axis_size("gyz")
    copies = jnp.broadcast_to(x[None], (n,) + x.shape)
    return jnp.sum(lax.all_to_all(copies, GY, 0, 0), axis=0)


def gy_max(x):
    return swap_combine(swap_combine(x, "gyz", jnp.maximum), "gyy", jnp.maximum)


def gy_sum_rows(x):
    part = exchange_scatter_sum(x, "gyy").astype(x.dtype)
    part = swap_combine(part, "gyz", jnp.add).astype(x.dtype)
    return exchange_gather(part, "gyy")


def partial_attend(query, keys, values, valid, distance, slopes, scale):
    scores = jnp.einsum("chd,phd->chp", query, keys, preferred_element_type=jnp.float32) * scale
    scores = scores - slopes[None, :, None] * distance.astype(jnp.float32)[:, None, :]
    scores = jnp.where(valid[:, None, :], scores, floor_score)
    highest = jnp.max(scores, axis=-1)
    weights = jnp.where(valid[:, None, :], jnp.exp(scores - highest[..., None]), 0.0)
    totals = jnp.sum(weights, axis=-1)
    accum = jnp.einsum(
        "chp,phd->chd", weights.astype(jnp.bfloat16), values, preferred_element_type=jnp.float32
    )
    return (highest, totals, accum)


def write_cache(fresh_rows, cache_block, positions, length, group):
    offset = positions - length
    inside = (offset >= 0) & (offset < group)
    block = cache_block.shape[0]
    padded = jnp.pad(fresh_rows, ((block, block), (0, 0), (0, 0)))
    start = jnp.clip(offset[0] + block, 0, group + block)
    taken = lax.dynamic_slice_in_dim(padded, start, block, axis=0)
    return jnp.where(inside[:, None, None], taken, cache_block)


def shards(hidden, ln_gain, w_qkv, w_out, kv_cache, cache_len):
    hidden_f = hidden.astype(jnp.float32)
    sums = gy_sum(jnp.stack([jnp.sum(hidden_f, axis=1), jnp.sum(hidden_f * hidden_f, axis=1)]))
    mean = sums[0] / D
    var = sums[1] / D - mean * mean
    normed = (
        (hidden_f - mean[:, None]) * lax.rsqrt(var + norm_eps)[:, None] * ln_gain[None, :]
    ).astype(jnp.bfloat16)
    local_heads = w_qkv.shape[1]
    head_size = w_qkv.shape[2] // 3
    weight_flat = w_qkv.reshape(w_qkv.shape[0], local_heads * 3 * head_size)
    partial_value = jnp.dot(
        ring_gather(normed, "gx"),
        weight_flat,
        preferred_element_type=jnp.float32,
    )
    requests = cache_len.shape[0]
    all_rows = partial_value.shape[0]
    group = all_rows // requests
    width_local = local_heads * head_size
    block = kv_cache.shape[1]
    positions = gy_index() * block + jnp.arange(block, dtype=jnp.int32)
    head_ids = lax.axis_index("gx") * local_heads + jnp.arange(local_heads, dtype=jnp.int32)
    all_heads = local_heads * lax.axis_size("gx")
    slopes = jnp.exp2(-8.0 * (head_ids + 1).astype(jnp.float32) / all_heads)
    scale = 1.0 / math.sqrt(head_size)
    steps_c = jnp.arange(group, dtype=jnp.int32)
    tops_list = []
    totals_list = []
    accum_list = []
    caches = []
    qkv = gy_sum_rows(partial_value.astype(jnp.bfloat16))
    qkv = qkv.reshape(requests, group, local_heads, 3 * head_size)
    fresh = jnp.stack(
        [
            qkv[:, :, :, head_size : 2 * head_size].reshape(requests, group, width_local),
            qkv[:, :, :, 2 * head_size :].reshape(requests, group, width_local),
        ],
        axis=2,
    )
    for request in range(requests):
        length = cache_len[request]
        updated = write_cache(fresh[request], kv_cache[request], positions, length, group)
        caches.append(updated)
        keys = updated[:, 0].reshape(block, local_heads, head_size)
        values = updated[:, 1].reshape(block, local_heads, head_size)
        distance = (length + steps_c)[:, None] - positions[None, :]
        part_top, part_total, part_accum = partial_attend(
            qkv[request, :, :, :head_size], keys, values, distance >= 0, distance, slopes, scale
        )
        tops_list.append(part_top)
        totals_list.append(part_total)
        accum_list.append(part_accum)
    tops = jnp.stack(tops_list)
    totals = jnp.stack(totals_list)
    accums = jnp.stack(accum_list)
    rows = requests * group
    packed = jnp.concatenate(
        [
            accums.astype(jnp.bfloat16).reshape(rows, width_local),
            totals.astype(jnp.bfloat16).reshape(rows, local_heads),
        ],
        axis=1,
    )
    attn = attend_combine(packed, tops.reshape(rows, local_heads), local_heads)
    projected = ring_scatter_sum(
        jnp.dot(attn, w_out, preferred_element_type=jnp.float32).astype(jnp.bfloat16), "gx"
    )
    mixed = (projected + hidden_f).astype(jnp.bfloat16)
    return (mixed, jnp.stack(caches))


def solution(mesh):
    n_gy = mesh.shape["gy"]
    split = Mesh(
        mesh.devices.reshape(mesh.shape["req"], mesh.shape["gx"], n_gy // 2, 2),
        ("req", "gx") + GY,
    )
    in_specs = (
        P(("req", "gx"), GY),
        P(GY),
        P(GY, "gx", None),
        P("gx", GY),
        P("req", GY, None, "gx"),
        P("req"),
    )
    out_specs = (P(("req", "gx"), GY), P("req", GY, None, "gx"))
    return jax.shard_map(shards, mesh=split, in_specs=in_specs, out_specs=out_specs, check_vma=False)
```
